32 devices in a mesh: groups: 2 (over y), tm: 4 (over z), space: 2 (over x), dp: 2 (over core).
Axes of the slice: x: 2, y: 2, z: 4, core: 2. Of those that a mesh axis runs over, the one named last changes fastest.
Arguments:
- video_input: bfloat16 [4, 4, 8, 256, 96], P(('groups', 'dp'), 'tm', 'space'), parts along dimension 0, may hold values from -48 to 48
- out_cotangent: bfloat16 [4, 4, 8, 256, 96], P(('groups', 'dp'), 'tm', 'space'), parts along dimension 0, may hold values from -6 to 6
- conv_weight: bfloat16 [3, 3, 3, 96, 96], replicated, may hold values from -0.125 to 0.125
- sketch_signs: int32 [2, 96, 32], replicated, may hold values from 0 to 1
Outputs:
- input_grad: bfloat16 [4, 4, 8, 256, 96], P(('groups', 'dp'), 'tm', 'space'), parts along dimension 0
- weight_grad: float32 [6, 3, 3, 96, 96], P('groups'), parts along dimension 0
- sketches: float32 [4, 96, 32], P('groups'), parts along dimension 0
The draws below stay inside these ranges and needn't reach their ends.
There are 2 independent parts, one for each index of `groups`. The reference program is written for one: setup_inputs(seed, part) draws one part's arguments, and reference() takes and returns one part's arrays. A program takes and returns all parts, laid end to end along the dimension named above; an argument that names none is the same for every part. Nothing has to cross between parts.
All inputs are finite; a program needn't handle non-finite values.
Results may differ from the reference program's by a relative error of at most 0.0025.
Values may be sent and summed in bfloat16 or wider, within the bound.
No kernel may reach another device: no remote copies, remote signals or barrier semaphores. Data moves between devices by JAX's collectives and lax.ppermute only.
A program may use at most 64 MiB of HBM per device.

```python
import jax
import jax.numpy as jnp
from jax import lax

C = 96
RANK = 32
COLS = 256
CLIPS = 2
FRAMES = 4
HEIGHT = 8


def draw_video_input(key, part):
    keys = jax.random.split(key, 3)
    shape = (CLIPS, FRAMES, HEIGHT, COLS, C)
    channel_scale = jnp.exp(jax.random.uniform(keys[0], (C,), minval=-1.15, maxval=1.15))
    pixel_scale = jnp.exp(jax.random.uniform(keys[1], (CLIPS, FRAMES, HEIGHT, COLS, 1), minval=-0.6, maxval=0.6))
    frame_pos = jnp.arange(FRAMES, dtype=jnp.float32) / float(max(FRAMES - 1, 1))
    ramp = jnp.power(3.0, frame_pos - 0.5)
    base = jax.random.normal(keys[2], shape)
    values = base * channel_scale * pixel_scale * ramp[None, :, None, None, None]
    return jnp.clip(values, -48.0, 48.0).astype(jnp.bfloat16)


def touch_ends(array, stream_key, smallest, top_value):
    dims = array.shape
    place = [jax.random.randint(jax.random.fold_in(stream_key, axis), (), 0, dims[axis]) for axis in range(len(dims))]
    array = array.at[tuple(place)].set(smallest)
    longest = dims.index(max(dims))
    place[longest] = (place[longest] + 1) % dims[longest]
    return array.at[tuple(place)].set(top_value)


def level_of(stream_key, extent, pieces, least, top_value):
    def one(axis_at, parts):
        heights = jax.random.uniform(jax.random.fold_in(jax.random.fold_in(stream_key, 6), axis_at), (parts,), jnp.float32, least / len(pieces), top_value / len(pieces))
        return jnp.repeat(jnp.exp(heights), extent[axis_at] // parts).reshape((-1,) + (1,) * (len(extent) - axis_at - 1))

    loudness = one(*pieces[0])
    for cut in pieces[1:]:
        loudness = loudness * one(*cut)
    return loudness


def gaussian(rng, extent, scale, limit, cuts=(), held_as=jnp.bfloat16):
    loudness = level_of(rng, extent, cuts, -0.22, 0.18) if cuts else 1.0
    values = jax.random.normal(rng, extent, jnp.float32) * scale * loudness
    return jnp.minimum(jnp.maximum(values, -limit), limit).astype(held_as)


def setup_inputs(seed: int = 0, part: int = 0) -> dict:
    streams_of = jax.random.split(jax.random.key(seed), 5)
    part_keys = jax.random.split(jax.random.fold_in(streams_of[4], part), 5)
    return {
        "video_input": draw_video_input(jax.random.fold_in(jax.random.fold_in(streams_of[4], part), 71), part),
        "out_cotangent": gaussian(part_keys[1], (CLIPS, FRAMES, HEIGHT, COLS, C), 1.0, 6.0, ((0, 2), (1, 4), (2, 2))),
        "conv_weight": gaussian(streams_of[2], (3, 3, 3, C, C), (27 * C) ** -0.5, 0.125),
        "sketch_signs": touch_ends(jax.random.randint(streams_of[3], (2, C, RANK), 0, 2), jax.random.fold_in(streams_of[3], 1), 0, 1).astype(jnp.int32),
    }


def reference(video_input, out_cotangent, conv_weight, sketch_signs):
    clips, frames, height, width, chans = video_input.shape
    pix = clips * frames * height * width
    xin = video_input.astype(jnp.float32)
    hidden = jax.nn.silu(xin).astype(jnp.bfloat16)
    grad_pad = jnp.pad(out_cotangent, ((0, 0), (0, 2), (1, 1), (1, 1), (0, 0)))
    hid_pad = jnp.pad(hidden, ((0, 0), (2, 0), (1, 1), (1, 1), (0, 0)))
    grad_flat = out_cotangent.reshape(pix, chans)
    hid_flat = hidden.reshape(pix, chans)
    grad_hidden = jnp.zeros((pix, chans), jnp.float32)
    kernel_terms = []
    for a in range(3):
        for b in range(3):
            for e in range(3):
                gwin = grad_pad[:, 2 - a:2 - a + frames, 2 - b:2 - b + height, 2 - e:2 - e + width].reshape(pix, chans)
                grad_hidden = grad_hidden + jnp.dot(gwin, conv_weight[a, b, e].T, preferred_element_type=jnp.float32)
                hwin = hid_pad[:, a:a + frames, b:b + height, e:e + width].reshape(pix, chans)
                kernel_terms.append(jnp.dot(hwin.T, grad_flat, preferred_element_type=jnp.float32))
    weight_grad = jnp.stack(kernel_terms).reshape(3, 3, 3, chans, chans) * (1.0 / jnp.sqrt(jnp.float32(pix)))
    sig = jax.nn.sigmoid(xin).reshape(pix, chans)
    xflat = xin.reshape(pix, chans)
    input_grad = (grad_hidden * sig * (1.0 + xflat * (1.0 - sig))).astype(jnp.bfloat16)
    input_grad = input_grad.reshape(clips, frames, height, width, chans)
    omega = (2 * sketch_signs - 1).astype(jnp.float32)
    cov_hidden = jnp.dot(hid_flat.T, hid_flat, preferred_element_type=jnp.float32)
    cov_grad = jnp.dot(grad_flat.T, grad_flat, preferred_element_type=jnp.float32)
    sketch_one = jnp.dot(cov_hidden, omega[0], precision=lax.Precision.HIGHEST)
    sketch_two = jnp.dot(cov_grad, omega[1], precision=lax.Precision.HIGHEST)
    sketches = jnp.stack([sketch_one, sketch_two]) / jnp.float32(pix)
    return (input_grad, weight_grad, sketches)
```

```python
import jax
import jax.numpy as jnp
from jax import lax
from jax.sharding import PartitionSpec as P


def padded(value, sides, width):
    for axis, dim in sides:
        peers, length = (lax.axis_size(axis), value.shape[dim])
        up = [(i, (i + 1) % peers) for i in range(peers - 1)]
        down = [(j, i) for i, j in up]
        last = lax.slice_in_dim(value, length - width, length, axis=dim)
        leading = lax.slice_in_dim(value, 0, width, axis=dim)
        before = lax.ppermute(last, axis, up)
        after = lax.ppermute(leading, axis, down)
        value = jnp.concatenate([before, value, after], axis=dim)
    return value


def passed_along(block, axis, distance):
    devices = range(lax.axis_size(axis))
    route = [(i - distance, i) for i in devices if i - distance in devices]
    return lax.ppermute(block, axis, route)


def exchanged(block, axis, distance):
    peers = lax.axis_size(axis)
    return lax.ppermute(block, axis, [(i, i ^ distance) for i in range(peers)])


def group_sum(flat, steps):
    kept = []
    for axis, distance in steps:
        upper = (lax.axis_index(axis) // distance) % 2 == 1
        half = flat.shape[0] // 2
        low, high = flat[:half], flat[half:]
        keep = jnp.where(upper, high, low)
        send = jnp.where(upper, low, high)
        flat = keep + exchanged(send, axis, distance)
        kept.append((axis, distance, upper))
    for axis, distance, upper in reversed(kept):
        other = exchanged(flat, axis, distance)
        flat = jnp.where(
            upper,
            jnp.concatenate([other, flat]),
            jnp.concatenate([flat, other]),
        )
    return flat


def halving_steps():
    steps = []
    for axis in ("dp", "space", "tm"):
        distance = 1
        while distance < lax.axis_size(axis):
            steps.append((axis, distance))
            distance *= 2
    return steps


def reduced_together(kernel_local, sketch_terms):
    axes = ("tm", "space", "dp")
    if any(lax.axis_size(a) & (lax.axis_size(a) - 1) for a in axes):
        return lax.psum(kernel_local, axes), lax.psum(sketch_terms, axes)
    steps = halving_steps()
    pieces = 2 ** len(steps)
    lanes = 128
    sizes = (kernel_local.size, sketch_terms.size)
    total = sum(sizes)
    rows = -(-total // (lanes * pieces)) * pieces
    flat = jnp.concatenate([kernel_local.reshape(-1), sketch_terms.reshape(-1)])
    flat = jnp.pad(flat, (0, rows * lanes - total)).reshape(rows, lanes)
    flat = group_sum(flat, steps).reshape(-1)
    kernel_total = flat[: sizes[0]].reshape(kernel_local.shape)
    sketch_total = flat[sizes[0] : total].reshape(sketch_terms.shape)
    return kernel_total, sketch_total


def silu_slope(value):
    sig = jax.nn.sigmoid(value)
    return sig * (1.0 + value * (1.0 - sig))


def pad_columns(field):
    return jnp.pad(field, ((0, 0), (0, 0), (1, 1), (0, 0)))


def contract_rows(left, right):
    return lax.dot_general(
        left, right, (((0,), (0,)), ((), ())), preferred_element_type=jnp.float32
    )


def on_device(video_input, out_cotangent, conv_weight, sketch_signs):
    xin = video_input[:, 0]
    grad_out = out_cotangent[:, 0]
    batch, rows, width, chans = xin.shape
    count = batch * rows * width
    hidden = jax.nn.silu(xin.astype(jnp.float32)).astype(jnp.bfloat16)
    hid_flat = hidden.reshape(count, chans)
    grad_flat = grad_out.reshape(count, chans)
    grad_rows = padded(grad_out, (("space", 1),), 1)
    grad_frames = [pad_columns(grad_rows)]
    for lag in (1, 2):
        grad_frames.append(pad_columns(passed_along(grad_rows, "tm", -lag)))
    hid_rows = padded(hidden, (("space", 1),), 1)
    hid_frames = [pad_columns(hid_rows)]
    for lag in (1, 2):
        hid_frames.append(pad_columns(passed_along(hid_rows, "tm", lag)))
    grad_hidden = jnp.zeros((count, chans), jnp.float32)
    kernel_terms = []
    for a in range(3):
        for b in range(3):
            source = grad_frames[2 - a]
            slab = jnp.concatenate(
                [source[:, 2 - b : 2 - b + rows, 2 - e : 2 - e + width, :] for e in range(3)],
                axis=-1,
            ).reshape(count, 3 * chans)
            weight_mat = jnp.transpose(conv_weight[a, b], (0, 2, 1)).reshape(3 * chans, chans)
            grad_hidden = grad_hidden + jnp.dot(
                slab, weight_mat, preferred_element_type=jnp.float32
            )
            earlier = hid_frames[2 - a]
            hid_slab = jnp.concatenate(
                [earlier[:, b : b + rows, e : e + width, :] for e in range(3)], axis=-1
            ).reshape(count, 3 * chans)
            kernel_terms.append(contract_rows(hid_slab, grad_flat).reshape(3, chans, chans))
    kernel_local = jnp.stack(kernel_terms).reshape(3, 3, 3, chans, chans)
    xflat = xin.reshape(count, chans).astype(jnp.float32)
    input_grad = (grad_hidden * silu_slope(xflat)).astype(jnp.bfloat16)
    input_grad = input_grad.reshape(batch, 1, rows, width, chans)
    omega = (2 * sketch_signs - 1).astype(jnp.float32)
    cov_hidden = contract_rows(hid_flat, hid_flat)
    cov_grad = contract_rows(grad_flat, grad_flat)
    sketch_terms = jnp.stack(
        [
            jnp.dot(cov_hidden, omega[0], precision=lax.Precision.HIGHEST),
            jnp.dot(cov_grad, omega[1], precision=lax.Precision.HIGHEST),
        ]
    )
    total_pixels = (
        count
        * video_input.shape[1]
        * lax.axis_size("tm")
        * lax.axis_size("space")
        * lax.axis_size("dp")
    )
    kernel_total, sketch_total = reduced_together(kernel_local, sketch_terms)
    sketches = sketch_total / jnp.float32(total_pixels)
    weight_grad = kernel_total * (1.0 / jnp.sqrt(jnp.float32(total_pixels)))
    return (input_grad, weight_grad, sketches)


def solution(mesh):
    in_specs = (
        P(("groups", "dp"), "tm", "space", None, None),
        P(("groups", "dp"), "tm", "space", None, None),
        P(),
        P(),
    )
    out_specs = (
        P(("groups", "dp"), "tm", "space", None, None),
        P("groups", None, None, None, None),
        P("groups", None, None),
    )
    return jax.shard_map(
        on_device, mesh=mesh, in_specs=in_specs, out_specs=out_specs, check_vma=False
    )
```

```python
import jax
import jax.numpy as jnp
from jax import lax
from jax.sharding import PartitionSpec as P


def padded(value, sides, width):
    for axis, dim in sides:
        peers, length = (lax.axis_size(axis), value.shape[dim])
        up = [(i, (i + 1) % peers) for i in range(peers - 1)]
        down = [(j, i) for i, j in up]
        last = lax.slice_in_dim(value, length - width, length, axis=dim)
        leading = lax.slice_in_dim(value, 0, width, axis=dim)
        before = lax.ppermute(last, axis, up)
        after = lax.ppermute(leading, axis, down)
        value = jnp.concatenate([before, value, after], axis=dim)
    return value


def passed_along(block, axis, distance):
    devices = range(lax.axis_size(axis))
    route = [(i - distance, i) for i in devices if i - distance in devices]
    return lax.ppermute(block, axis, route)


def exchanged(block, axis, distance):
    peers = lax.axis_size(axis)
    return lax.ppermute(block, axis, [(i, i ^ distance) for i in range(peers)])


def group_sum(flat, steps):
    kept = []
    for axis, distance in steps:
        upper = (lax.axis_index(axis) // distance) % 2 == 1
        half = flat.shape[0] // 2
        low, high = flat[:half], flat[half:]
        keep = jnp.where(upper, high, low)
        send = jnp.where(upper, low, high)
        flat = keep + exchanged(send, axis, distance)
        kept.append((axis, distance, upper))
    for axis, distance, upper in reversed(kept):
        other = exchanged(flat, axis, distance)
        flat = jnp.where(
            upper,
            jnp.concatenate([other, flat]),
            jnp.concatenate([flat, other]),
        )
    return flat


def halving_steps():
    steps = []
    for axis in ("dp", "space", "tm"):
        distance = 1
        while distance < lax.axis_size(axis):
            steps.append((axis, distance))
            distance *= 2
    return steps


def reduced_together(kernel_local, sketch_terms):
    axes = ("tm", "space", "dp")
    if any(lax.axis_size(a) & (lax.axis_size(a) - 1) for a in axes):
        return lax.psum(kernel_local, axes), lax.psum(sketch_terms, axes)
    steps = halving_steps()
    pieces = 2 ** len(steps)
    lanes = 128
    sizes = (kernel_local.size, sketch_terms.size)
    total = sum(sizes)
    rows = -(-total // (lanes * pieces)) * pieces
    flat = jnp.concatenate([kernel_local.reshape(-1), sketch_terms.reshape(-1)])
    flat = jnp.pad(flat, (0, rows * lanes - total)).reshape(rows, lanes)
    flat = group_sum(flat, steps).reshape(-1)
    kernel_total = flat[: sizes[0]].reshape(kernel_local.shape)
    sketch_total = flat[sizes[0] : total].reshape(sketch_terms.shape)
    return kernel_total, sketch_total


def silu_slope(value):
    sig = jax.nn.sigmoid(value)
    return sig * (1.0 + value * (1.0 - sig))


def pad_columns(field):
    return jnp.pad(field, ((0, 0), (0, 0), (1, 1), (0, 0)))


def contract_rows(left, right):
    return lax.dot_general(
        left, right, (((0,), (0,)), ((), ())), preferred_element_type=jnp.float32
    )


def on_device(video_input, out_cotangent, conv_weight, sketch_signs):
    xin = video_input[:, 0]
    grad_out = out_cotangent[:, 0]
    batch, rows, width, chans = xin.shape
    count = batch * rows * width
    hidden = jax.nn.silu(xin.astype(jnp.float32)).astype(jnp.bfloat16)
    hid_flat = hidden.reshape(count, chans)
    grad_flat = grad_out.reshape(count, chans)
    grad_rows = padded(grad_out, (("space", 1),), 1)
    grad_frames = [pad_columns(grad_rows)]
    for lag in (1, 2):
        grad_frames.append(pad_columns(passed_along(grad_rows, "tm", -lag)))
    grad_hidden = jnp.zeros((count, chans), jnp.float32)
    kernel_terms = []
    for a in range(3):
        for b in range(3):
            source = grad_frames[2 - a]
            slab = jnp.concatenate(
                [source[:, 2 - b : 2 - b + rows, 2 - e : 2 - e + width, :] for e in range(3)],
                axis=-1,
            ).reshape(count, 3 * chans)
            weight_mat = jnp.transpose(conv_weight[a, b], (0, 2, 1)).reshape(3 * chans, chans)
            grad_hidden = grad_hidden + jnp.dot(
                slab, weight_mat, preferred_element_type=jnp.float32
            )
            term = contract_rows(hid_flat, slab).reshape(chans, 3, chans)
            kernel_terms.append(jnp.transpose(term, (1, 0, 2)))
    kernel_local = jnp.stack(kernel_terms).reshape(3, 3, 3, chans, chans)
    xflat = xin.reshape(count, chans).astype(jnp.float32)
    input_grad = (grad_hidden * silu_slope(xflat)).astype(jnp.bfloat16)
    input_grad = input_grad.reshape(batch, 1, rows, width, chans)
    omega = (2 * sketch_signs - 1).astype(jnp.float32)
    cov_hidden = contract_rows(hid_flat, hid_flat)
    cov_grad = contract_rows(grad_flat, grad_flat)
    sketch_terms = jnp.stack(
        [
            jnp.dot(cov_hidden, omega[0], precision=lax.Precision.HIGHEST),
            jnp.dot(cov_grad, omega[1], precision=lax.Precision.HIGHEST),
        ]
    )
    total_pixels = (
        count
        * video_input.shape[1]
        * lax.axis_size("tm")
        * lax.axis_size("space")
        * lax.axis_size("dp")
    )
    kernel_total, sketch_total = reduced_together(kernel_local, sketch_terms)
    sketches = sketch_total / jnp.float32(total_pixels)
    weight_grad = kernel_total * (1.0 / jnp.sqrt(jnp.float32(total_pixels)))
    return (input_grad, weight_grad, sketches)


def solution(mesh):
    in_specs = (
        P(("groups", "dp"), "tm", "space", None, None),
        P(("groups", "dp"), "tm", "space", None, None),
        P(),
        P(),
    )
    out_specs = (
        P(("groups", "dp"), "tm", "space", None, None),
        P("groups", None, None, None, None),
        P("groups", None, None),
    )
    return jax.shard_map(
        on_device, mesh=mesh, in_specs=in_specs, out_specs=out_specs, check_vma=False
    )
```

```python
import jax
import jax.numpy as jnp
from jax import lax
from jax.sharding import PartitionSpec as P


def padded(value, sides, width):
    for axis, dim in sides:
        peers, length = (lax.axis_size(axis), value.shape[dim])
        up = [(i, (i + 1) % peers) for i in range(peers - 1)]
        down = [(j, i) for i, j in up]
        last = lax.slice_in_dim(value, length - width, length, axis=dim)
        leading = lax.slice_in_dim(value, 0, width, axis=dim)
        before = lax.ppermute(last, axis, up)
        after = lax.ppermute(leading, axis, down)
        value = jnp.concatenate([before, value, after], axis=dim)
    return value


def passed_along(block, axis, distance):
    devices = range(lax.axis_size(axis))
    route = [(i - distance, i) for i in devices if i - distance in devices]
    return lax.ppermute(block, axis, route)


def exchanged(block, axis, distance):
    peers = lax.axis_size(axis)
    return lax.ppermute(block, axis, [(i, i ^ distance) for i in range(peers)])


def group_sum(flat, steps):
    kept = []
    for axis, distance in steps:
        upper = (lax.axis_index(axis) // distance) % 2 == 1
        half = flat.shape[0] // 2
        low, high = flat[:half], flat[half:]
        keep = jnp.where(upper, high, low)
        send = jnp.where(upper, low, high)
        flat = keep + exchanged(send, axis, distance)
        kept.append((axis, distance, upper))
    for axis, distance, upper in reversed(kept):
        other = exchanged(flat, axis, distance)
        flat = jnp.where(
            upper,
            jnp.concatenate([other, flat]),
            jnp.concatenate([flat, other]),
        )
    return flat


def halving_steps():
    steps = []
    for axis in ("dp", "space", "tm"):
        distance = 1
        while distance < lax.axis_size(axis):
            steps.append((axis, distance))
            distance *= 2
    return steps


def reduced_together(kernel_local, sketch_terms):
    axes = ("tm", "space", "dp")
    if any(lax.axis_size(a) & (lax.axis_size(a) - 1) for a in axes):
        return lax.psum(kernel_local, axes), lax.psum(sketch_terms, axes)
    steps = halving_steps()
    pieces = 2 ** len(steps)
    lanes = 128
    sizes = (kernel_local.size, sketch_terms.size)
    total = sum(sizes)
    rows = -(-total // (lanes * pieces)) * pieces
    flat = jnp.concatenate([kernel_local.reshape(-1), sketch_terms.reshape(-1)])
    flat = jnp.pad(flat, (0, rows * lanes - total)).reshape(rows, lanes)
    flat = group_sum(flat, steps).reshape(-1)
    kernel_total = flat[: sizes[0]].reshape(kernel_local.shape)
    sketch_total = flat[sizes[0] : total].reshape(sketch_terms.shape)
    return kernel_total, sketch_total


def from_neighbour(block, frames_ahead, rows_ahead):
    frames, rows = lax.axis_size("tm"), lax.axis_size("space")
    route = []
    for t in range(frames):
        for r in range(rows):
            source = (t + frames_ahead, r + rows_ahead)
            if 0 <= source[0] < frames and 0 <= source[1] < rows:
                route.append((source[0] * rows + source[1], t * rows + r))
    return lax.ppermute(block, ("tm", "space"), route)


def cotangent_frames(grad_out):
    result = []
    for ahead in range(3):
        centre = grad_out if ahead == 0 else from_neighbour(grad_out, ahead, 0)
        above = from_neighbour(grad_out[:, -1:], ahead, -1)
        below = from_neighbour(grad_out[:, :1], ahead, 1)
        result.append(pad_columns(jnp.concatenate([above, centre, below], axis=1)))
    return result


def silu_slope(value):
    sig = jax.nn.sigmoid(value)
    return sig * (1.0 + value * (1.0 - sig))


def pad_columns(field):
    return jnp.pad(field, ((0, 0), (0, 0), (1, 1), (0, 0)))


def contract_rows(left, right):
    return lax.dot_general(
        left, right, (((0,), (0,)), ((), ())), preferred_element_type=jnp.float32
    )


def on_device(video_input, out_cotangent, conv_weight, sketch_signs):
    xin = video_input[:, 0]
    grad_out = out_cotangent[:, 0]
    batch, rows, width, chans = xin.shape
    count = batch * rows * width
    hidden = jax.nn.silu(xin.astype(jnp.float32)).astype(jnp.bfloat16)
    hid_flat = hidden.reshape(count, chans)
    grad_flat = grad_out.reshape(count, chans)
    grad_frames = cotangent_frames(grad_out)
    grad_hidden = jnp.zeros((count, chans), jnp.float32)
    flipped = jnp.swapaxes(conv_weight, 3, 4)
    kernel_terms = []
    for a in range(3):
        for b in range(3):
            source = grad_frames[2 - a]
            slab = jnp.concatenate(
                [source[:, 2 - b : 2 - b + rows, 2 - e : 2 - e + width, :] for e in range(3)],
                axis=-1,
            ).reshape(count, 3 * chans)
            grad_hidden = grad_hidden + jnp.dot(
                slab, flipped[a, b].reshape(3 * chans, chans), preferred_element_type=jnp.float32
            )
            term = contract_rows(hid_flat, slab).reshape(chans, 3, chans)
            kernel_terms.append(jnp.transpose(term, (1, 0, 2)))
    kernel_local = jnp.stack(kernel_terms).reshape(3, 3, 3, chans, chans)
    xflat = xin.reshape(count, chans).astype(jnp.float32)
    input_grad = (grad_hidden * silu_slope(xflat)).astype(jnp.bfloat16)
    input_grad = input_grad.reshape(batch, 1, rows, width, chans)
    omega = (2 * sketch_signs - 1).astype(jnp.float32)
    cov_hidden = contract_rows(hid_flat, hid_flat)
    cov_grad = contract_rows(grad_flat, grad_flat)
    sketch_terms = jnp.stack(
        [
            jnp.dot(cov_hidden, omega[0], precision=lax.Precision.HIGHEST),
            jnp.dot(cov_grad, omega[1], precision=lax.Precision.HIGHEST),
        ]
    )
    total_pixels = (
        count
        * video_input.shape[1]
        * lax.axis_size("tm")
        * lax.axis_size("space")
        * lax.axis_size("dp")
    )
    kernel_total, sketch_total = reduced_together(kernel_local, sketch_terms)
    sketches = sketch_total / jnp.float32(total_pixels)
    weight_grad = kernel_total * (1.0 / jnp.sqrt(jnp.float32(total_pixels)))
    return (input_grad, weight_grad, sketches)


def solution(mesh):
    in_specs = (
        P(("groups", "dp"), "tm", "space", None, None),
        P(("groups", "dp"), "tm", "space", None, None),
        P(),
        P(),
    )
    out_specs = (
        P(("groups", "dp"), "tm", "space", None, None),
        P("groups", None, None, None, None),
        P("groups", None, None),
    )
    return jax.shard_map(
        on_device, mesh=mesh, in_specs=in_specs, out_specs=out_specs, check_vma=False
    )
```

```python
import jax
import jax.numpy as jnp
from jax import lax
from jax.sharding import PartitionSpec as P


def padded(value, sides, width):
    for axis, dim in sides:
        peers, length = (lax.axis_size(axis), value.shape[dim])
        up = [(i, (i + 1) % peers) for i in range(peers - 1)]
        down = [(j, i) for i, j in up]
        last = lax.slice_in_dim(value, length - width, length, axis=dim)
        leading = lax.slice_in_dim(value, 0, width, axis=dim)
        before = lax.ppermute(last, axis, up)
        after = lax.ppermute(leading, axis, down)
        value = jnp.concatenate([before, value, after], axis=dim)
    return value


def passed_along(block, axis, distance):
    devices = range(lax.axis_size(axis))
    route = [(i - distance, i) for i in devices if i - distance in devices]
    return lax.ppermute(block, axis, route)


def exchanged(block, axis, distance):
    peers = lax.axis_size(axis)
    return lax.ppermute(block, axis, [(i, i ^ distance) for i in range(peers)])


def group_index(axes):
    index = 0
    for axis in axes:
        index = index * lax.axis_size(axis) + lax.axis_index(axis)
    return index


def group_size(axes):
    size = 1
    for axis in axes:
        size *= lax.axis_size(axis)
    return size


def direct_scatter(flat, axes):
    peers, me = group_size(axes), group_index(axes)
    piece = flat.shape[0] // peers
    chunk = lambda at: lax.dynamic_slice_in_dim(flat, (at % peers) * piece, piece)
    total = chunk(me)
    for shift in range(1, peers):
        route = [(i, (i + shift) % peers) for i in range(peers)]
        total = total + lax.ppermute(chunk(me + shift), axes, route)
    return total


def direct_gather(piece, axes):
    peers, me = group_size(axes), group_index(axes)
    held = [piece]
    for shift in range(1, peers):
        route = [(i, (i + shift) % peers) for i in range(peers)]
        held.append(lax.ppermute(piece, axes, route))
    ordered = jnp.concatenate([held[0]] + held[:0:-1])
    doubled = jnp.concatenate([ordered, ordered])
    start = ((peers - me) % peers) * piece.shape[0]
    return lax.dynamic_slice_in_dim(doubled, start, ordered.shape[0])


def halving_scatter(flat, axis, distance):
    upper = (lax.axis_index(axis) // distance) % 2 == 1
    half = flat.shape[0] // 2
    low, high = flat[:half], flat[half:]
    keep = jnp.where(upper, high, low)
    send = jnp.where(upper, low, high)
    return keep + exchanged(send, axis, distance)


def halving_gather(flat, axis, distance):
    upper = (lax.axis_index(axis) // distance) % 2 == 1
    other = exchanged(flat, axis, distance)
    return jnp.where(
        upper, jnp.concatenate([other, flat]), jnp.concatenate([flat, other])
    )


def reduction_steps():
    steps = [("halve", "dp", d) for d in halving_distances("dp")]
    steps.extend(("halve", "space", d) for d in halving_distances("space"))
    if lax.axis_size("tm") <= 4:
        steps.append(("direct", ("tm",), 0))
    else:
        steps.extend(("halve", "tm", d) for d in halving_distances("tm"))
    return steps


def halving_distances(axis):
    distances, distance = [], 1
    while distance < lax.axis_size(axis):
        distances.append(distance)
        distance *= 2
    return distances


def step_pieces(step):
    kind, axes, _ = step
    return group_size(axes) if kind == "direct" else 2


def group_sum(flat, steps):
    for kind, axes, distance in steps:
        if kind == "direct":
            flat = direct_scatter(flat, axes)
        else:
            flat = halving_scatter(flat, axes, distance)
    for kind, axes, distance in reversed(steps):
        if kind == "direct":
            flat = direct_gather(flat, axes)
        else:
            flat = halving_gather(flat, axes, distance)
    return flat


def reduced_together(kernel_local, sketch_terms):
    axes = ("tm", "space", "dp")
    if any(lax.axis_size(a) & (lax.axis_size(a) - 1) for a in axes):
        return lax.psum(kernel_local, axes), lax.psum(sketch_terms, axes)
    steps = reduction_steps()
    pieces = 1
    for step in steps:
        pieces *= step_pieces(step)
    lanes = 128
    sizes = (kernel_local.size, sketch_terms.size)
    total = sum(sizes)
    rows = -(-total // (lanes * pieces)) * pieces
    flat = jnp.concatenate([kernel_local.reshape(-1), sketch_terms.reshape(-1)])
    flat = jnp.pad(flat, (0, rows * lanes - total)).reshape(rows, lanes)
    flat = group_sum(flat, steps).reshape(-1)
    kernel_total = flat[: sizes[0]].reshape(kernel_local.shape)
    sketch_total = flat[sizes[0] : total].reshape(sketch_terms.shape)
    return kernel_total, sketch_total


def from_neighbour(block, frames_ahead, rows_ahead):
    frames, rows = lax.axis_size("tm"), lax.axis_size("space")
    route = []
    for t in range(frames):
        for r in range(rows):
            source = (t + frames_ahead, r + rows_ahead)
            if 0 <= source[0] < frames and 0 <= source[1] < rows:
                route.append((source[0] * rows + source[1], t * rows + r))
    return lax.ppermute(block, ("tm", "space"), route)


def cotangent_frames(grad_out):
    result = []
    for ahead in range(3):
        centre = grad_out if ahead == 0 else from_neighbour(grad_out, ahead, 0)
        above = from_neighbour(grad_out[:, -1:], ahead, -1)
        below = from_neighbour(grad_out[:, :1], ahead, 1)
        result.append(pad_columns(jnp.concatenate([above, centre, below], axis=1)))
    return result


def silu_slope(value):
    sig = jax.nn.sigmoid(value)
    return sig * (1.0 + value * (1.0 - sig))


def pad_columns(field):
    return jnp.pad(field, ((0, 0), (0, 0), (1, 1), (0, 0)))


def contract_rows(left, right):
    return lax.dot_general(
        left, right, (((0,), (0,)), ((), ())), preferred_element_type=jnp.float32
    )


def on_device(video_input, out_cotangent, conv_weight, sketch_signs):
    xin = video_input[:, 0]
    grad_out = out_cotangent[:, 0]
    batch, rows, width, chans = xin.shape
    count = batch * rows * width
    hidden = jax.nn.silu(xin.astype(jnp.float32)).astype(jnp.bfloat16)
    hid_flat = hidden.reshape(count, chans)
    grad_flat = grad_out.reshape(count, chans)
    grad_frames = cotangent_frames(grad_out)
    grad_hidden = jnp.zeros((count, chans), jnp.float32)
    flipped = jnp.swapaxes(conv_weight, 3, 4)
    kernel_terms = []
    for a in range(3):
        for b in range(3):
            source = grad_frames[2 - a]
            slab = jnp.concatenate(
                [source[:, 2 - b : 2 - b + rows, 2 - e : 2 - e + width, :] for e in range(3)],
                axis=-1,
            ).reshape(count, 3 * chans)
            grad_hidden = grad_hidden + jnp.dot(
                slab, flipped[a, b].reshape(3 * chans, chans), preferred_element_type=jnp.float32
            )
            term = contract_rows(hid_flat, slab).reshape(chans, 3, chans)
            kernel_terms.append(jnp.transpose(term, (1, 0, 2)))
    kernel_local = jnp.stack(kernel_terms).reshape(3, 3, 3, chans, chans)
    xflat = xin.reshape(count, chans).astype(jnp.float32)
    input_grad = (grad_hidden * silu_slope(xflat)).astype(jnp.bfloat16)
    input_grad = input_grad.reshape(batch, 1, rows, width, chans)
    omega = (2 * sketch_signs - 1).astype(jnp.float32)
    cov_hidden = contract_rows(hid_flat, hid_flat)
    cov_grad = contract_rows(grad_flat, grad_flat)
    sketch_terms = jnp.stack(
        [
            jnp.dot(cov_hidden, omega[0], precision=lax.Precision.HIGHEST),
            jnp.dot(cov_grad, omega[1], precision=lax.Precision.HIGHEST),
        ]
    )
    total_pixels = (
        count
        * video_input.shape[1]
        * lax.axis_size("tm")
        * lax.axis_size("space")
        * lax.axis_size("dp")
    )
    kernel_total, sketch_total = reduced_together(kernel_local, sketch_terms)
    sketches = sketch_total / jnp.float32(total_pixels)
    weight_grad = kernel_total * (1.0 / jnp.sqrt(jnp.float32(total_pixels)))
    return (input_grad, weight_grad, sketches)


def solution(mesh):
    in_specs = (
        P(("groups", "dp"), "tm", "space", None, None),
        P(("groups", "dp"), "tm", "space", None, None),
        P(),
        P(),
    )
    out_specs = (
        P(("groups", "dp"), "tm", "space", None, None),
        P("groups", None, None, None, None),
        P("groups", None, None),
    )
    return jax.shard_map(
        on_device, mesh=mesh, in_specs=in_specs, out_specs=out_specs, check_vma=False
    )
```

```python
import jax
import jax.numpy as jnp
from jax import lax
from jax.sharding import PartitionSpec as P


def padded(value, sides, width):
    for axis, dim in sides:
        peers, length = (lax.axis_size(axis), value.shape[dim])
        up = [(i, (i + 1) % peers) for i in range(peers - 1)]
        down = [(j, i) for i, j in up]
        last = lax.slice_in_dim(value, length - width, length, axis=dim)
        leading = lax.slice_in_dim(value, 0, width, axis=dim)
        before = lax.ppermute(last, axis, up)
        after = lax.ppermute(leading, axis, down)
        value = jnp.concatenate([before, value, after], axis=dim)
    return value


def passed_along(block, axis, distance):
    devices = range(lax.axis_size(axis))
    route = [(i - distance, i) for i in devices if i - distance in devices]
    return lax.ppermute(block, axis, route)


def exchanged(block, axis, distance):
    peers = lax.axis_size(axis)
    return lax.ppermute(block, axis, [(i, i ^ distance) for i in range(peers)])


def group_index(axes):
    index = 0
    for axis in axes:
        index = index * lax.axis_size(axis) + lax.axis_index(axis)
    return index


def group_size(axes):
    size = 1
    for axis in axes:
        size *= lax.axis_size(axis)
    return size


def direct_scatter(flat, axes):
    peers, me = group_size(axes), group_index(axes)
    piece = flat.shape[0] // peers
    chunk = lambda at: lax.dynamic_slice_in_dim(flat, (at % peers) * piece, piece)
    total = chunk(me)
    for shift in range(1, peers):
        route = [(i, (i + shift) % peers) for i in range(peers)]
        total = total + lax.ppermute(chunk(me + shift), axes, route)
    return total


def direct_gather(piece, axes):
    peers, me = group_size(axes), group_index(axes)
    held = [piece]
    for shift in range(1, peers):
        route = [(i, (i + shift) % peers) for i in range(peers)]
        held.append(lax.ppermute(piece, axes, route))
    ordered = jnp.concatenate([held[0]] + held[:0:-1])
    doubled = jnp.concatenate([ordered, ordered])
    start = ((peers - me) % peers) * piece.shape[0]
    return lax.dynamic_slice_in_dim(doubled, start, ordered.shape[0])


def halving_scatter(flat, axis, distance):
    upper = (lax.axis_index(axis) // distance) % 2 == 1
    half = flat.shape[0] // 2
    low, high = flat[:half], flat[half:]
    keep = jnp.where(upper, high, low)
    send = jnp.where(upper, low, high)
    return keep + exchanged(send, axis, distance)


def halving_gather(flat, axis, distance):
    upper = (lax.axis_index(axis) // distance) % 2 == 1
    other = exchanged(flat, axis, distance)
    return jnp.where(
        upper, jnp.concatenate([other, flat]), jnp.concatenate([flat, other])
    )


def reduction_steps():
    steps = [("halve", "dp", d) for d in halving_distances("dp")]
    steps.extend(("halve", "space", d) for d in halving_distances("space"))
    if lax.axis_size("tm") <= 4:
        steps.append(("direct", ("tm",), 0))
    else:
        steps.extend(("halve", "tm", d) for d in halving_distances("tm"))
    return steps


def halving_distances(axis):
    distances, distance = [], 1
    while distance < lax.axis_size(axis):
        distances.append(distance)
        distance *= 2
    return distances


def step_pieces(step):
    kind, axes, _ = step
    return group_size(axes) if kind == "direct" else 2


def group_sum(flat, steps):
    for kind, axes, distance in steps:
        if kind == "direct":
            flat = direct_scatter(flat, axes)
        else:
            flat = halving_scatter(flat, axes, distance)
    for kind, axes, distance in reversed(steps):
        if kind == "direct":
            flat = direct_gather(flat, axes)
        else:
            flat = halving_gather(flat, axes, distance)
    return flat


def reduced_together(kernel_local, sketch_terms):
    axes = ("tm", "space", "dp")
    if any(lax.axis_size(a) & (lax.axis_size(a) - 1) for a in axes):
        return lax.psum(kernel_local, axes), lax.psum(sketch_terms, axes)
    steps = reduction_steps()
    pieces = 1
    for step in steps:
        pieces *= step_pieces(step)
    lanes = 128
    sizes = (kernel_local.size, sketch_terms.size)
    total = sum(sizes)
    rows = -(-total // (lanes * pieces)) * pieces
    flat = jnp.concatenate([kernel_local.reshape(-1), sketch_terms.reshape(-1)])
    flat = jnp.pad(flat, (0, rows * lanes - total)).reshape(rows, lanes)
    flat = group_sum(flat, steps).reshape(-1)
    kernel_total = flat[: sizes[0]].reshape(kernel_local.shape)
    sketch_total = flat[sizes[0] : total].reshape(sketch_terms.shape)
    return kernel_total, sketch_total


def from_neighbour(block, frames_ahead, rows_ahead):
    frames, rows = lax.axis_size("tm"), lax.axis_size("space")
    route = []
    for t in range(frames):
        for r in range(rows):
            source = (t + frames_ahead, r + rows_ahead)
            if 0 <= source[0] < frames and 0 <= source[1] < rows:
                route.append((source[0] * rows + source[1], t * rows + r))
    return lax.ppermute(block, ("tm", "space"), route)


def edge_rows(grad_out, ahead):
    if lax.axis_size("space") != 2:
        return from_neighbour(grad_out[:, -1:], ahead, -1), from_neighbour(grad_out[:, :1], ahead, 1)
    frames = lax.axis_size("tm")
    lower = lax.axis_index("space") == 0
    edge = jnp.where(lower, grad_out[:, -1:], grad_out[:, :1])
    route = [
        ((t + ahead) * 2 + r, t * 2 + 1 - r)
        for t in range(frames)
        for r in range(2)
        if t + ahead < frames
    ]
    arrived = lax.ppermute(edge, ("tm", "space"), route)
    empty = jnp.zeros_like(arrived)
    return jnp.where(lower, empty, arrived), jnp.where(lower, arrived, empty)


def cotangent_frames(grad_out):
    result = []
    for ahead in range(3):
        centre = grad_out if ahead == 0 else from_neighbour(grad_out, ahead, 0)
        above, below = edge_rows(grad_out, ahead)
        result.append(pad_columns(jnp.concatenate([above, centre, below], axis=1)))
    return result


def silu_slope(value):
    sig = jax.nn.sigmoid(value)
    return sig * (1.0 + value * (1.0 - sig))


def pad_columns(field):
    return jnp.pad(field, ((0, 0), (0, 0), (1, 1), (0, 0)))


def contract_rows(left, right):
    return lax.dot_general(
        left, right, (((0,), (0,)), ((), ())), preferred_element_type=jnp.float32
    )


def on_device(video_input, out_cotangent, conv_weight, sketch_signs):
    xin = video_input[:, 0]
    grad_out = out_cotangent[:, 0]
    batch, rows, width, chans = xin.shape
    count = batch * rows * width
    hidden = jax.nn.silu(xin.astype(jnp.float32)).astype(jnp.bfloat16)
    hid_flat = hidden.reshape(count, chans)
    grad_flat = grad_out.reshape(count, chans)
    grad_frames = cotangent_frames(grad_out)
    grad_hidden = jnp.zeros((count, chans), jnp.float32)
    flipped = jnp.swapaxes(conv_weight, 3, 4)
    kernel_terms = []
    for a in range(3):
        for b in range(3):
            source = grad_frames[2 - a]
            slab = jnp.concatenate(
                [source[:, 2 - b : 2 - b + rows, 2 - e : 2 - e + width, :] for e in range(3)],
                axis=-1,
            ).reshape(count, 3 * chans)
            grad_hidden = grad_hidden + jnp.dot(
                slab, flipped[a, b].reshape(3 * chans, chans), preferred_element_type=jnp.float32
            )
            term = contract_rows(hid_flat, slab).reshape(chans, 3, chans)
            kernel_terms.append(jnp.transpose(term, (1, 0, 2)))
    kernel_local = jnp.stack(kernel_terms).reshape(3, 3, 3, chans, chans)
    xflat = xin.reshape(count, chans).astype(jnp.float32)
    input_grad = (grad_hidden * silu_slope(xflat)).astype(jnp.bfloat16)
    input_grad = input_grad.reshape(batch, 1, rows, width, chans)
    omega = (2 * sketch_signs - 1).astype(jnp.float32)
    cov_hidden = contract_rows(hid_flat, hid_flat)
    cov_grad = contract_rows(grad_flat, grad_flat)
    sketch_terms = jnp.stack(
        [
            jnp.dot(cov_hidden, omega[0], precision=lax.Precision.HIGHEST),
            jnp.dot(cov_grad, omega[1], precision=lax.Precision.HIGHEST),
        ]
    )
    total_pixels = (
        count
        * video_input.shape[1]
        * lax.axis_size("tm")
        * lax.axis_size("space")
        * lax.axis_size("dp")
    )
    kernel_total, sketch_total = reduced_together(kernel_local, sketch_terms)
    sketches = sketch_total / jnp.float32(total_pixels)
    weight_grad = kernel_total * (1.0 / jnp.sqrt(jnp.float32(total_pixels)))
    return (input_grad, weight_grad, sketches)


def solution(mesh):
    in_specs = (
        P(("groups", "dp"), "tm", "space", None, None),
        P(("groups", "dp"), "tm", "space", None, None),
        P(),
        P(),
    )
    out_specs = (
        P(("groups", "dp"), "tm", "space", None, None),
        P("groups", None, None, None, None),
        P("groups", None, None),
    )
    return jax.shard_map(
        on_device, mesh=mesh, in_specs=in_specs, out_specs=out_specs, check_vma=False
    )
```
